512 devices in a mesh: section: 32 (over x, z), expert: 16 (over y, core).
Axes of the slice: x: 4, y: 8, z: 8, core: 2. Of those that a mesh axis runs over, the one named last changes fastest.
Arguments:
- tokens: bfloat16 [32, 3072, 1024], P('section', 'expert'), may hold values from -6 to 6
- out_grad: bfloat16 [32, 3072, 1024], P('section', 'expert'), may hold values from -6 to 6
- expert_ids: int32 [32, 3072, 2], P('section', 'expert'), may hold values from 0 to 15, all different within a row; in each aligned block of 192 rows (0 to 191, 192 to 383, ..., all dimensions but the last counted through in order) at most 48 rows name the same one
- gate_weights: float32 [32, 3072, 2], P('section', 'expert'), may hold values from 0.2 to 1
- w_gate: bfloat16 [32, 16, 1024, 256], P('section', 'expert'), may hold values from -0.1875 to 0.1875
- w_up: bfloat16 [32, 16, 1024, 256], P('section', 'expert'), may hold values from -0.1875 to 0.1875
- w_down: bfloat16 [32, 16, 256, 1024], P('section', 'expert'), may hold values from -0.25 to 0.25
Outputs:
- token_grad: bfloat16 [32, 3072, 1024], P('section', 'expert')
- grad_gate: bfloat16 [32, 16, 1024, 256], P('section', 'expert')
- grad_up: bfloat16 [32, 16, 1024, 256], P('section', 'expert')
- grad_down: bfloat16 [32, 16, 256, 1024], P('section', 'expert')
The draws below stay inside these ranges and needn't reach their ends.
Inputs may be any that keep to these rules, and one draw needn't show every extreme that they name: `expert_ids`: each token names 2 different experts. Among the 192 tokens of one device (aligned blocks of rows of one section) no expert is named by more than 48 (token, choice) pairs, a bound that some block reaches.
All inputs are finite; a program needn't handle non-finite values.
Results may differ from the reference program's by a relative error of at most 0.009.
Values may be sent and summed in bfloat16 or wider, within the bound.
No kernel may reach another device: no remote copies, remote signals or barrier semaphores. Data moves between devices by JAX's collectives and lax.ppermute only.
A program may use at most 64 MiB of HBM per device.

```python
import math
import jax
import jax.numpy as jnp
import numpy as np
from jax import lax

D = 1024
H = 512
TOPK = 2
TOK_DEV = 192
HH = 256
EXPERTS = 16
TOKENS = 3072
CAP = 48
N_SECTION = 32
N_EXPERT = 16


def block_levels(rng, dims, shards, smallest, largest):
    def one(position, parts):
        draws = jax.random.uniform(jax.random.fold_in(jax.random.fold_in(rng, 6), position), (parts,), jnp.float32, smallest / len(shards), largest / len(shards))
        return jnp.repeat(jnp.exp(draws), dims[position] // parts).reshape((-1,) + (1,) * (len(dims) - position - 1))

    loudness = one(*shards[0])
    for cut in shards[1:]:
        loudness = loudness * one(*cut)
    return loudness


def deal_out(key, own, number, rows, amount, top, most, slope):
    ranking = jax.random.permutation(key, amount)
    crowded, common = portions_of(amount, rows * top, most, slope, True), portions_of(amount, rows * top, most, slope, False)
    places = jnp.arange(amount)

    def named(lengths, offset_by):
        used = int((lengths > 0).sum())
        fixed = max(1, used // 4)
        passed = fixed + (places - fixed + offset_by * (used - fixed)) % max(1, amount - fixed)
        return jnp.zeros((amount,), jnp.int32).at[ranking[jnp.where(places < fixed, places, passed)]].set(jnp.asarray(lengths, jnp.int32))

    lengths = jnp.where(number % 4 == 0, named(crowded, number // 4), named(common, number - number // 4 - 1))
    mixed = jax.random.permutation(jax.random.fold_in(own, 3), amount)
    donor, receiver = mixed[0:amount // 2 * 2:2], mixed[1:amount // 2 * 2:2]
    room = jnp.minimum(lengths[donor] - 1, most - lengths[receiver]) // 2
    room = jnp.where((donor == ranking[0]) | (receiver == ranking[0]) | (lengths[receiver] == 0), 0, jnp.maximum(room, 0))
    passed = jax.random.randint(jax.random.fold_in(own, 4), (amount // 2,), 0, 1 << 20) % (room + 1)
    lengths = lengths.at[donor].add(-passed).at[receiver].add(passed)
    items = jnp.searchsorted(jnp.cumsum(lengths), jnp.arange(rows * top), side="right").astype(jnp.int32)
    grid = items.reshape(top, rows).T
    grid = grid[jax.random.permutation(jax.random.fold_in(own, 1), rows)]
    offset_by = jax.random.randint(jax.random.fold_in(own, 2), (rows, 1), 0, top)
    return jnp.take_along_axis(grid, (jnp.arange(top)[None, :] + offset_by) % top, axis=1)


def portions_of(number_of, total, reach, lean, full):
    portions = [(1 << 20) // math.isqrt(grade ** lean) + 1 for grade in range(1, number_of + 1)]
    largest = reach if full else min(reach, max(-(-total // number_of), total * portions[0] // sum(portions)))
    least = 1 if total - largest >= number_of - 1 else 0
    counts, spare = [largest] + [least] * (number_of - 1), total - largest - least * (number_of - 1)
    while spare > 0:
        candidates = [i for i in range(1, number_of) if counts[i] < largest] or [i for i in range(1, number_of) if counts[i] < reach]
        mass, budget = sum([portions[i] for i in candidates]), spare
        for i in candidates:
            more = min(reach - counts[i], max(1, budget * portions[i] // mass), spare)
            counts[i] = counts[i] + more
            spare = spare - more
    return np.array(counts)


def noise(own_key, dims, scale, most, split=(), kind=jnp.bfloat16):
    level = block_levels(own_key, dims, split, -0.22, 0.18) if split else 1.0
    values = jax.random.normal(own_key, dims, jnp.float32) * scale * level
    return jnp.minimum(jnp.maximum(values, -most), most).astype(kind)


def setup_inputs(seed: int = 0) -> dict:
    keys = jax.random.split(jax.random.key(seed), 8)
    tokens = noise(keys[0], (N_SECTION, TOKENS, D), 1.0, 6.0, ((0, 32), (1, 16)))
    out_grad = noise(keys[1], (N_SECTION, TOKENS, D), 1.0, 6.0, ((0, 32), (1, 16)))
    expert_ids_keys = jax.random.split(jax.random.fold_in(keys[2], 1), N_SECTION * TOKENS // TOK_DEV)
    expert_ids_turns = jax.random.permutation(jax.random.fold_in(keys[2], 3), N_SECTION * TOKENS // TOK_DEV)
    expert_ids = jax.vmap(lambda own, number: deal_out(jax.random.fold_in(keys[2], 2), own, number, TOK_DEV, EXPERTS, TOPK, CAP, 2))(expert_ids_keys, expert_ids_turns).reshape((N_SECTION, TOKENS, TOPK))
    gate_weights = jnp.clip(0.2 + 0.8 * jax.random.uniform(keys[3], (N_SECTION, TOKENS, TOPK), jnp.float32) ** block_levels(keys[3], (N_SECTION, TOKENS, TOPK), ((0, 32), (1, 16)), -0.2, 0.2), 0.2, 1.0)
    w_gate = noise(keys[4], (N_SECTION, EXPERTS, D, HH), D ** -0.5, 0.1875, ((0, 32), (1, 16)))
    w_up = noise(keys[5], (N_SECTION, EXPERTS, D, HH), D ** -0.5, 0.1875, ((0, 32), (1, 16)))
    w_down = noise(keys[6], (N_SECTION, EXPERTS, HH, D), H ** -0.5, 0.25, ((0, 32), (1, 16)))
    return dict(tokens=tokens, out_grad=out_grad, expert_ids=expert_ids, gate_weights=gate_weights, w_gate=w_gate, w_up=w_up, w_down=w_down)


def make_slots(ids, gates, inputs, grads, cap, experts):
    tok, topk = ids.shape
    width = inputs.shape[1]
    count = tok * topk
    flat = ids.reshape(count)
    onehot = (flat[:, None] == jnp.arange(experts, dtype=jnp.int32)[None, :]).astype(jnp.int32)
    before = jnp.cumsum(onehot, axis=0) - onehot
    rank = lax.optimization_barrier(jnp.sum(before * onehot, axis=1)).astype(jnp.int32)
    slot = (flat * cap + rank).astype(jnp.int32)
    source = jnp.full((experts * cap,), count, jnp.int32).at[slot].set(jnp.arange(count, dtype=jnp.int32))
    token = (source // topk).astype(jnp.int32)
    padded_in = jnp.concatenate([inputs, jnp.zeros((1, width), inputs.dtype)], axis=0)
    scaled = (gates.astype(jnp.float32)[:, :, None] * grads.astype(jnp.float32)[:, None, :]).astype(jnp.bfloat16)
    padded_grad = jnp.concatenate([scaled.reshape(count, width), jnp.zeros((1, width), jnp.bfloat16)], axis=0)
    slot_in = padded_in[token].reshape(experts, cap, width)
    slot_grad = padded_grad[source].reshape(experts, cap, width)
    live = (source < count).reshape(experts, cap)
    return (slot_in, slot_grad, live, slot)

def unslot(slot_rows, slot, tok, topk):
    width = slot_rows.shape[-1]
    picked = slot_rows[slot].astype(jnp.float32).reshape(tok, topk, width)
    return lax.optimization_barrier(jnp.sum(picked, axis=1)).astype(jnp.bfloat16)

def expert_grads(rows_in, rows_grad, gate_w, up_w, down_w):
    contract_last = (((1,), (1,)), ((), ()))
    contract_rows = (((0,), (0,)), ((), ()))
    gate_pre = jnp.dot(rows_in, gate_w, preferred_element_type=jnp.float32)
    up_pre = jnp.dot(rows_in, up_w, preferred_element_type=jnp.float32)
    sigmoid_g = jax.nn.sigmoid(gate_pre)
    swish_val = gate_pre * sigmoid_g
    act = (swish_val * up_pre).astype(jnp.bfloat16)
    act_grad = lax.dot_general(rows_grad, down_w, contract_last, preferred_element_type=jnp.float32)
    gate_grad = (act_grad * up_pre * sigmoid_g * (1.0 + gate_pre * (1.0 - sigmoid_g))).astype(jnp.bfloat16)
    up_grad = (act_grad * swish_val).astype(jnp.bfloat16)
    pair_grad = lax.dot_general(gate_grad, gate_w, contract_last, preferred_element_type=jnp.float32)
    pair_grad = pair_grad + lax.dot_general(up_grad, up_w, contract_last, preferred_element_type=jnp.float32)
    grad_g = lax.dot_general(rows_in, gate_grad, contract_rows, preferred_element_type=jnp.float32)
    grad_u = lax.dot_general(rows_in, up_grad, contract_rows, preferred_element_type=jnp.float32)
    grad_d = lax.dot_general(act, rows_grad, contract_rows, preferred_element_type=jnp.float32)
    return (pair_grad, grad_g, grad_u, grad_d)

def reference(tokens, out_grad, expert_ids, gate_weights, w_gate, w_up, w_down):
    pairs = N_SECTION // 2
    blocks = 2 * N_EXPERT
    scale = 1.0 / math.sqrt(2 * TOPK * TOK_DEV)

    def one_pair(index):
        other = index + pairs

        def both(array):
            return jnp.stack([array[index], array[other]])
        x_all = both(tokens).reshape(blocks, TOK_DEV, D)
        dy_all = both(out_grad).reshape(blocks, TOK_DEV, D)
        ids_all = both(expert_ids).reshape(blocks, TOK_DEV, TOPK)
        gw_all = both(gate_weights).reshape(blocks, TOK_DEV, TOPK)

        def slots_of(ids, gates, inputs, grads):
            return make_slots(ids, gates, inputs, grads, CAP, EXPERTS)
        slot_in, slot_grad, live, slot = jax.vmap(slots_of)(ids_all, gw_all, x_all, dy_all)
        x_exp = jnp.transpose(slot_in, (1, 0, 2, 3)).reshape(EXPERTS, blocks * CAP, D)
        dy_exp = jnp.transpose(slot_grad, (1, 0, 2, 3)).reshape(EXPERTS, blocks * CAP, D)
        full_gate = jnp.concatenate([w_gate[index], w_gate[other]], axis=2)
        full_up = jnp.concatenate([w_up[index], w_up[other]], axis=2)
        full_down = jnp.concatenate([w_down[index], w_down[other]], axis=1)

        def per_expert(items):
            return expert_grads(items[0], items[1], items[2], items[3], items[4])
        pair_grad, grad_g, grad_u, grad_d = lax.map(per_expert, (x_exp, dy_exp, full_gate, full_up, full_down))
        back = pair_grad.astype(jnp.bfloat16).reshape(EXPERTS, blocks, CAP, D)
        back = jnp.transpose(back, (1, 0, 2, 3)).reshape(blocks, EXPERTS * CAP, D)

        def unslot_one(rows, where_to):
            return unslot(rows, where_to, TOK_DEV, TOPK)
        token_part = jax.vmap(unslot_one)(back, slot).reshape(2, TOKENS, D)
        grad_g = (grad_g * scale).astype(jnp.bfloat16)
        grad_u = (grad_u * scale).astype(jnp.bfloat16)
        grad_d = (grad_d * scale).astype(jnp.bfloat16)
        gate_two = jnp.stack([grad_g[:, :, :HH], grad_g[:, :, HH:]])
        up_two = jnp.stack([grad_u[:, :, :HH], grad_u[:, :, HH:]])
        down_two = jnp.stack([grad_d[:, :HH, :], grad_d[:, HH:, :]])
        return (token_part, gate_two, up_two, down_two)
    token_all, gate_all, up_all, down_all = lax.map(one_pair, jnp.arange(pairs, dtype=jnp.int32))

    def arrange(array):
        moved = jnp.swapaxes(array, 0, 1)
        return moved.reshape((N_SECTION,) + moved.shape[2:])
    return (arrange(token_all), arrange(gate_all), arrange(up_all), arrange(down_all))
```

```python
import math

import jax
import jax.numpy as jnp
from jax import lax
from jax.sharding import PartitionSpec as P

CHUNKS = 2


def partner(value, axis, bit):
    mask = 2**bit
    pairs = [(source, source ^ mask) for source in range(lax.axis_size(axis))]
    return lax.ppermute(value, axis, pairs)


def dispatch_matrix(ids, cap, experts):
    tok, topk = ids.shape
    count = tok * topk
    flat = ids.reshape(count)
    onehot = (flat[:, None] == jnp.arange(experts, dtype=jnp.int32)[None, :]).astype(jnp.int32)
    before = jnp.cumsum(onehot, axis=0) - onehot
    rank = jnp.sum(before * onehot, axis=1)
    slot = flat * cap + rank
    hit = slot[None, :] == jnp.arange(experts * cap, dtype=jnp.int32)[:, None]
    return hit


def expert_grads(rows_in, rows_grad, gate_w, up_w, down_w):
    contract_last = (((1,), (1,)), ((), ()))
    contract_rows = (((0,), (0,)), ((), ()))
    gate_pre = jnp.dot(rows_in, gate_w, preferred_element_type=jnp.float32)
    up_pre = jnp.dot(rows_in, up_w, preferred_element_type=jnp.float32)
    sigmoid_g = jax.nn.sigmoid(gate_pre)
    swish_val = gate_pre * sigmoid_g
    act = (swish_val * up_pre).astype(jnp.bfloat16)
    act_grad = lax.dot_general(rows_grad, down_w, contract_last, preferred_element_type=jnp.float32)
    gate_grad = (act_grad * up_pre * sigmoid_g * (1.0 + gate_pre * (1.0 - sigmoid_g))).astype(
        jnp.bfloat16
    )
    up_grad = (act_grad * swish_val).astype(jnp.bfloat16)
    pair_grad = lax.dot_general(
        gate_grad, gate_w, contract_last, preferred_element_type=jnp.float32
    )
    pair_grad = pair_grad + lax.dot_general(
        up_grad, up_w, contract_last, preferred_element_type=jnp.float32
    )
    grad_g = lax.dot_general(rows_in, gate_grad, contract_rows, preferred_element_type=jnp.float32)
    grad_u = lax.dot_general(rows_in, up_grad, contract_rows, preferred_element_type=jnp.float32)
    grad_d = lax.dot_general(act, rows_grad, contract_rows, preferred_element_type=jnp.float32)
    return (pair_grad, grad_g, grad_u, grad_d)


def per_device(tokens, out_grad, expert_ids, gate_weights, w_gate, w_up, w_down):
    inputs = tokens[0]
    grads = out_grad[0]
    ids = expert_ids[0]
    gates = gate_weights[0]
    tok, topk = ids.shape
    width = inputs.shape[1]
    experts = lax.axis_size("expert")
    cap = 2 * topk * tok // experts
    scale = 1.0 / math.sqrt(2 * topk * tok)
    pair_bit = lax.axis_size("section").bit_length() - 2

    own_gate = w_gate[0, 0]
    own_up = w_up[0, 0]
    own_down = w_down[0, 0]
    half = own_gate.shape[1]
    other_gate, other_up, other_down = partner((own_gate, own_up, own_down), "section", pair_bit)

    hit = dispatch_matrix(ids, cap, experts)
    pair_gate = jnp.sum(jnp.where(hit, gates.reshape(tok * topk)[None, :], 0.0), axis=1)
    token_hit = hit.reshape(experts * cap, tok, topk).any(axis=2).astype(jnp.bfloat16)
    both = jnp.concatenate([inputs, grads], axis=1)

    token_hit = token_hit.reshape(experts, cap, tok)
    pair_gate = pair_gate.reshape(experts, cap)
    step = cap // CHUNKS
    chunk_rows = experts * step

    full_gate = full_up = full_down = None
    token_acc = jnp.zeros((tok, width), jnp.float32)
    acc_g = acc_u = acc_d = None
    for c in range(CHUNKS):
        sel = token_hit[:, c * step:(c + 1) * step, :].reshape(chunk_rows, tok)
        sgate = pair_gate[:, c * step:(c + 1) * step].reshape(chunk_rows, 1)
        picked = jnp.dot(sel, both, preferred_element_type=jnp.float32)
        slot_in = picked[:, :width].astype(jnp.bfloat16)
        slot_grad = (picked[:, width:] * sgate).astype(jnp.bfloat16)
        send = jnp.concatenate([slot_in, slot_grad], axis=1).reshape(experts, step, 2 * width)
        recv = lax.all_to_all(send, "expert", split_axis=0, concat_axis=0, tiled=True)
        recv = recv.reshape(chunk_rows, 2 * width)
        if full_gate is None:
            full_gate = jnp.concatenate([own_gate, other_gate], axis=1)
            full_up = jnp.concatenate([own_up, other_up], axis=1)
            full_down = jnp.concatenate([own_down, other_down], axis=0)
        pair_grad, grad_g, grad_u, grad_d = expert_grads(
            recv[:, :width], recv[:, width:], full_gate, full_up, full_down
        )
        if acc_g is None:
            acc_g, acc_u, acc_d = grad_g, grad_u, grad_d
        else:
            acc_g, acc_u, acc_d = acc_g + grad_g, acc_u + grad_u, acc_d + grad_d
        back = pair_grad.astype(jnp.bfloat16).reshape(experts, step, width)
        home = lax.all_to_all(back, "expert", split_axis=0, concat_axis=0, tiled=True)
        home = home.reshape(chunk_rows, width)
        token_acc = token_acc + lax.dot_general(
            sel, home, (((0,), (0,)), ((), ())), preferred_element_type=jnp.float32
        )

    peer_g, peer_u, peer_d = partner(
        (
            acc_g[:, half:].astype(jnp.bfloat16),
            acc_u[:, half:].astype(jnp.bfloat16),
            acc_d[half:, :].astype(jnp.bfloat16),
        ),
        "section",
        pair_bit,
    )
    mine_g = acc_g[:, :half] + peer_g.astype(jnp.float32)
    mine_u = acc_u[:, :half] + peer_u.astype(jnp.float32)
    mine_d = acc_d[:half, :] + peer_d.astype(jnp.float32)
    token_grad = token_acc.astype(jnp.bfloat16)
    out_g = (mine_g * scale).astype(jnp.bfloat16)
    out_u = (mine_u * scale).astype(jnp.bfloat16)
    out_d = (mine_d * scale).astype(jnp.bfloat16)
    return (token_grad[None], out_g[None, None], out_u[None, None], out_d[None, None])


def solution(mesh):
    in_specs = (
        P("section", "expert", None),
        P("section", "expert", None),
        P("section", "expert", None),
        P("section", "expert", None),
        P("section", "expert", None, None),
        P("section", "expert", None, None),
        P("section", "expert", None, None),
    )
    out_specs = (
        P("section", "expert", None),
        P("section", "expert", None, None),
        P("section", "expert", None, None),
        P("section", "expert", None, None),
    )
    return jax.shard_map(
        per_device, mesh=mesh, in_specs=in_specs, out_specs=out_specs, check_vma=False
    )
```

```python
import math

import jax
import jax.numpy as jnp
from jax import lax
from jax.sharding import PartitionSpec as P

CHUNKS = 2


def partner(value, axis, bit):
    mask = 2**bit
    pairs = [(source, source ^ mask) for source in range(lax.axis_size(axis))]
    return lax.ppermute(value, axis, pairs)


def dispatch_matrix(ids, cap, experts):
    tok, topk = ids.shape
    count = tok * topk
    flat = ids.reshape(count)
    onehot = (flat[:, None] == jnp.arange(experts, dtype=jnp.int32)[None, :]).astype(jnp.int32)
    before = jnp.cumsum(onehot, axis=0) - onehot
    rank = jnp.sum(before * onehot, axis=1)
    slot = flat * cap + rank
    hit = slot[None, :] == jnp.arange(experts * cap, dtype=jnp.int32)[:, None]
    return hit


def expert_grads(rows_in, rows_grad, gate_w, up_w, down_w):
    contract_last = (((1,), (1,)), ((), ()))
    contract_rows = (((0,), (0,)), ((), ()))
    gate_pre = jnp.dot(rows_in, gate_w, preferred_element_type=jnp.float32)
    up_pre = jnp.dot(rows_in, up_w, preferred_element_type=jnp.float32)
    sigmoid_g = jax.nn.sigmoid(gate_pre)
    swish_val = gate_pre * sigmoid_g
    act = (swish_val * up_pre).astype(jnp.bfloat16)
    act_grad = lax.dot_general(rows_grad, down_w, contract_last, preferred_element_type=jnp.float32)
    gate_grad = (act_grad * up_pre * sigmoid_g * (1.0 + gate_pre * (1.0 - sigmoid_g))).astype(
        jnp.bfloat16
    )
    up_grad = (act_grad * swish_val).astype(jnp.bfloat16)
    pair_grad = lax.dot_general(
        gate_grad, gate_w, contract_last, preferred_element_type=jnp.float32
    )
    pair_grad = pair_grad + lax.dot_general(
        up_grad, up_w, contract_last, preferred_element_type=jnp.float32
    )
    grad_g = lax.dot_general(rows_in, gate_grad, contract_rows, preferred_element_type=jnp.float32)
    grad_u = lax.dot_general(rows_in, up_grad, contract_rows, preferred_element_type=jnp.float32)
    grad_d = lax.dot_general(act, rows_grad, contract_rows, preferred_element_type=jnp.float32)
    return (pair_grad, grad_g, grad_u, grad_d)


def per_device(tokens, out_grad, expert_ids, gate_weights, w_gate, w_up, w_down):
    inputs = tokens[0]
    grads = out_grad[0]
    ids = expert_ids[0]
    gates = gate_weights[0]
    tok, topk = ids.shape
    width = inputs.shape[1]
    experts = lax.axis_size("expert")
    cap = 2 * topk * tok // experts
    scale = 1.0 / math.sqrt(2 * topk * tok)
    pair_bit = lax.axis_size("section").bit_length() - 2

    own_gate = w_gate[0, 0]
    own_up = w_up[0, 0]
    own_down = w_down[0, 0]
    dim, half = own_gate.shape
    packed = jnp.stack([own_gate, own_up, own_down.reshape(dim, half)])
    other = partner(packed, "section", pair_bit)
    full_gate = jnp.concatenate([own_gate, other[0]], axis=1)
    full_up = jnp.concatenate([own_up, other[1]], axis=1)
    full_down = jnp.concatenate([own_down, other[2].reshape(half, dim)], axis=0)

    hit = dispatch_matrix(ids, cap, experts)
    pair_gate = jnp.sum(jnp.where(hit, gates.reshape(tok * topk)[None, :], 0.0), axis=1)
    token_hit = hit.reshape(experts * cap, tok, topk).any(axis=2).astype(jnp.bfloat16)
    both = jnp.concatenate([inputs, grads], axis=1)

    token_hit = token_hit.reshape(experts, cap, tok)
    pair_gate = pair_gate.reshape(experts, cap)
    step = cap // CHUNKS
    chunk_rows = experts * step

    recv_all = []
    for c in range(CHUNKS):
        sel = token_hit[:, c * step:(c + 1) * step, :].reshape(chunk_rows, tok)
        sgate = pair_gate[:, c * step:(c + 1) * step].reshape(chunk_rows, 1)
        picked = jnp.dot(sel, both, preferred_element_type=jnp.float32)
        slot_in = picked[:, :width].astype(jnp.bfloat16)
        slot_grad = (picked[:, width:] * sgate).astype(jnp.bfloat16)
        send = jnp.concatenate([slot_in, slot_grad], axis=1).reshape(experts, step, 2 * width)
        recv = lax.all_to_all(send, "expert", split_axis=0, concat_axis=0, tiled=True)
        recv_all.append(recv)

    acc_g = acc_u = acc_d = None
    backs = []
    for c in range(CHUNKS):
        recv = recv_all[c].reshape(chunk_rows, 2 * width)
        pair_grad, grad_g, grad_u, grad_d = expert_grads(
            recv[:, :width], recv[:, width:], full_gate, full_up, full_down
        )
        if acc_g is None:
            acc_g, acc_u, acc_d = grad_g, grad_u, grad_d
        else:
            acc_g, acc_u, acc_d = acc_g + grad_g, acc_u + grad_u, acc_d + grad_d
        backs.append(pair_grad.astype(jnp.bfloat16).reshape(experts, step, width))

    back = jnp.concatenate(backs, axis=1)
    home = lax.all_to_all(back, "expert", split_axis=0, concat_axis=0, tiled=True)
    home = home.reshape(experts * cap, width)
    token_acc = lax.dot_general(
        token_hit.reshape(experts * cap, tok), home, (((0,), (0,)), ((), ())),
        preferred_element_type=jnp.float32,
    )

    peer_packed = jnp.stack(
        [
            acc_g[:, half:].astype(jnp.bfloat16),
            acc_u[:, half:].astype(jnp.bfloat16),
            acc_d[half:, :].astype(jnp.bfloat16).reshape(dim, half),
        ]
    )
    peer = partner(peer_packed, "section", pair_bit).astype(jnp.float32)
    mine_g = acc_g[:, :half] + peer[0]
    mine_u = acc_u[:, :half] + peer[1]
    mine_d = acc_d[:half, :] + peer[2].reshape(half, dim)
    token_grad = token_acc.astype(jnp.bfloat16)
    out_g = (mine_g * scale).astype(jnp.bfloat16)
    out_u = (mine_u * scale).astype(jnp.bfloat16)
    out_d = (mine_d * scale).astype(jnp.bfloat16)
    return (token_grad[None], out_g[None, None], out_u[None, None], out_d[None, None])


def solution(mesh):
    in_specs = (
        P("section", "expert", None),
        P("section", "expert", None),
        P("section", "expert", None),
        P("section", "expert", None),
        P("section", "expert", None, None),
        P("section", "expert", None, None),
        P("section", "expert", None, None),
    )
    out_specs = (
        P("section", "expert", None),
        P("section", "expert", None, None),
        P("section", "expert", None, None),
        P("section", "expert", None, None),
    )
    return jax.shard_map(
        per_device, mesh=mesh, in_specs=in_specs, out_specs=out_specs, check_vma=False
    )
```

```python
import math

import jax
import jax.numpy as jnp
from jax import lax
from jax.sharding import PartitionSpec as P


CHUNKS = 2


def partner(value, axis, bit):
    mask = 2**bit
    pairs = [(source, source ^ mask) for source in range(lax.axis_size(axis))]
    return lax.ppermute(value, axis, pairs)


def dispatch_matrix(ids, cap, experts):
    tok, topk = ids.shape
    count = tok * topk
    flat = ids.reshape(count)
    onehot = (flat[:, None] == jnp.arange(experts, dtype=jnp.int32)[None, :]).astype(jnp.int32)
    before = jnp.cumsum(onehot, axis=0) - onehot
    rank = jnp.sum(before * onehot, axis=1)
    slot = flat * cap + rank
    hit = slot[None, :] == jnp.arange(experts * cap, dtype=jnp.int32)[:, None]
    return hit


def grad_terms(rows_in, rows_grad, gate_w, up_w, down_w):
    contract_last = (((1,), (1,)), ((), ()))
    contract_rows = (((0,), (0,)), ((), ()))
    gate_pre = jnp.dot(rows_in, gate_w, preferred_element_type=jnp.float32)
    up_pre = jnp.dot(rows_in, up_w, preferred_element_type=jnp.float32)
    sigmoid_g = jax.nn.sigmoid(gate_pre)
    swish_val = gate_pre * sigmoid_g
    act = (swish_val * up_pre).astype(jnp.bfloat16)
    act_grad = lax.dot_general(rows_grad, down_w, contract_last, preferred_element_type=jnp.float32)
    gate_grad = (act_grad * up_pre * sigmoid_g * (1.0 + gate_pre * (1.0 - sigmoid_g))).astype(
        jnp.bfloat16
    )
    up_grad = (act_grad * swish_val).astype(jnp.bfloat16)

    def weight_part(lo, hi):
        return (
            lax.dot_general(rows_in, gate_grad[:, lo:hi], contract_rows, preferred_element_type=jnp.float32),
            lax.dot_general(rows_in, up_grad[:, lo:hi], contract_rows, preferred_element_type=jnp.float32),
            lax.dot_general(act[:, lo:hi], rows_grad, contract_rows, preferred_element_type=jnp.float32),
        )

    def pair_part():
        pair_grad = lax.dot_general(
            gate_grad, gate_w, contract_last, preferred_element_type=jnp.float32
        )
        pair_grad = pair_grad + lax.dot_general(
            up_grad, up_w, contract_last, preferred_element_type=jnp.float32
        )
        return pair_grad

    return weight_part, pair_part


def per_device(tokens, out_grad, expert_ids, gate_weights, w_gate, w_up, w_down):
    inputs = tokens[0]
    grads = out_grad[0]
    ids = expert_ids[0]
    gates = gate_weights[0]
    tok, topk = ids.shape
    width = inputs.shape[1]
    experts = lax.axis_size("expert")
    cap = 2 * topk * tok // experts
    scale = 1.0 / math.sqrt(2 * topk * tok)
    pair_bit = lax.axis_size("section").bit_length() - 2

    own_gate = w_gate[0, 0]
    own_up = w_up[0, 0]
    own_down = w_down[0, 0]
    dim, half = own_gate.shape
    packed = jnp.stack([own_gate, own_up, own_down.reshape(dim, half)])
    other = partner(packed, "section", pair_bit)
    full_gate = jnp.concatenate([own_gate, other[0]], axis=1)
    full_up = jnp.concatenate([own_up, other[1]], axis=1)
    full_down = jnp.concatenate([own_down, other[2].reshape(half, dim)], axis=0)

    hit = dispatch_matrix(ids, cap, experts)
    pair_gate = jnp.sum(jnp.where(hit, gates.reshape(tok * topk)[None, :], 0.0), axis=1)
    token_hit = hit.reshape(experts * cap, tok, topk).any(axis=2).astype(jnp.bfloat16)
    both = jnp.concatenate([inputs, grads], axis=1)

    token_hit = token_hit.reshape(experts, cap, tok)
    pair_gate = pair_gate.reshape(experts, cap)
    step = cap // CHUNKS
    chunk_rows = experts * step

    recv_all = []
    sels = []
    for c in range(CHUNKS):
        sel = token_hit[:, c * step:(c + 1) * step, :].reshape(chunk_rows, tok)
        sgate = pair_gate[:, c * step:(c + 1) * step].reshape(chunk_rows, 1)
        picked = jnp.dot(sel, both, preferred_element_type=jnp.float32)
        slot_in = picked[:, :width].astype(jnp.bfloat16)
        slot_grad = (picked[:, width:] * sgate).astype(jnp.bfloat16)
        send = jnp.concatenate([slot_in, slot_grad], axis=1).reshape(experts, step, 2 * width)
        recv = lax.all_to_all(send, "expert", split_axis=0, concat_axis=0, tiled=True)
        recv_all.append(recv)
        sels.append(sel)

    peer_acc = own_acc = None
    token_acc = None
    for c in range(CHUNKS):
        recv = recv_all[c].reshape(chunk_rows, 2 * width)
        weight_part, pair_part = grad_terms(
            recv[:, :width], recv[:, width:], full_gate, full_up, full_down
        )
        peer_terms = weight_part(half, 2 * half)
        if peer_acc is not None:
            peer_terms = tuple(a + b for a, b in zip(peer_acc, peer_terms))
        peer_acc = peer_terms
        back = pair_part().astype(jnp.bfloat16).reshape(experts, step, width)
        home = lax.all_to_all(back, "expert", split_axis=0, concat_axis=0, tiled=True)
        own_terms = weight_part(0, half)
        own_acc = own_terms if own_acc is None else tuple(a + b for a, b in zip(own_acc, own_terms))
        part = lax.dot_general(
            sels[c], home.reshape(chunk_rows, width), (((0,), (0,)), ((), ())),
            preferred_element_type=jnp.float32,
        )
        token_acc = part if token_acc is None else token_acc + part

    peer_g, peer_u, peer_d = peer_acc
    peer_packed = jnp.stack(
        [
            peer_g.astype(jnp.bfloat16),
            peer_u.astype(jnp.bfloat16),
            peer_d.astype(jnp.bfloat16).reshape(dim, half),
        ]
    )
    peer = partner(peer_packed, "section", pair_bit).astype(jnp.float32)
    own_g, own_u, own_d = own_acc
    mine_g = own_g + peer[0]
    mine_u = own_u + peer[1]
    mine_d = own_d + peer[2].reshape(half, dim)
    token_grad = token_acc.astype(jnp.bfloat16)
    out_g = (mine_g * scale).astype(jnp.bfloat16)
    out_u = (mine_u * scale).astype(jnp.bfloat16)
    out_d = (mine_d * scale).astype(jnp.bfloat16)
    return (token_grad[None], out_g[None, None], out_u[None, None], out_d[None, None])


def solution(mesh):
    in_specs = (
        P("section", "expert", None),
        P("section", "expert", None),
        P("section", "expert", None),
        P("section", "expert", None),
        P("section", "expert", None, None),
        P("section", "expert", None, None),
        P("section", "expert", None, None),
    )
    out_specs = (
        P("section", "expert", None),
        P("section", "expert", None, None),
        P("section", "expert", None, None),
        P("section", "expert", None, None),
    )
    return jax.shard_map(
        per_device, mesh=mesh, in_specs=in_specs, out_specs=out_specs, check_vma=False
    )
```

```python
import math

import jax
import jax.numpy as jnp
from jax import lax
from jax.sharding import PartitionSpec as P


def partner(value, axis, bit):
    mask = 2**bit
    pairs = [(source, source ^ mask) for source in range(lax.axis_size(axis))]
    return lax.ppermute(value, axis, pairs)


def dispatch_matrix(ids, cap, experts):
    tok, topk = ids.shape
    count = tok * topk
    flat = ids.reshape(count)
    onehot = (flat[:, None] == jnp.arange(experts, dtype=jnp.int32)[None, :]).astype(jnp.int32)
    before = jnp.cumsum(onehot, axis=0) - onehot
    rank = jnp.sum(before * onehot, axis=1)
    slot = flat * cap + rank
    hit = slot[None, :] == jnp.arange(experts * cap, dtype=jnp.int32)[:, None]
    return hit


def expert_grads(rows_in, rows_grad, gate_w, up_w, down_w):
    contract_last = (((1,), (1,)), ((), ()))
    contract_rows = (((0,), (0,)), ((), ()))
    gate_pre = jnp.dot(rows_in, gate_w, preferred_element_type=jnp.float32)
    up_pre = jnp.dot(rows_in, up_w, preferred_element_type=jnp.float32)
    sigmoid_g = jax.nn.sigmoid(gate_pre)
    swish_val = gate_pre * sigmoid_g
    act = (swish_val * up_pre).astype(jnp.bfloat16)
    act_grad = lax.dot_general(rows_grad, down_w, contract_last, preferred_element_type=jnp.float32)
    gate_grad = (act_grad * up_pre * sigmoid_g * (1.0 + gate_pre * (1.0 - sigmoid_g))).astype(
        jnp.bfloat16
    )
    up_grad = (act_grad * swish_val).astype(jnp.bfloat16)
    pair_grad = lax.dot_general(
        gate_grad, gate_w, contract_last, preferred_element_type=jnp.float32
    )
    pair_grad = pair_grad + lax.dot_general(
        up_grad, up_w, contract_last, preferred_element_type=jnp.float32
    )
    grad_g = lax.dot_general(rows_in, gate_grad, contract_rows, preferred_element_type=jnp.float32)
    grad_u = lax.dot_general(rows_in, up_grad, contract_rows, preferred_element_type=jnp.float32)
    grad_d = lax.dot_general(act, rows_grad, contract_rows, preferred_element_type=jnp.float32)
    return (pair_grad, grad_g, grad_u, grad_d)


def per_device(tokens, out_grad, expert_ids, gate_weights, w_gate, w_up, w_down):
    inputs = tokens[0]
    grads = out_grad[0]
    ids = expert_ids[0]
    gates = gate_weights[0]
    tok, topk = ids.shape
    width = inputs.shape[1]
    experts = lax.axis_size("expert")
    cap = 2 * topk * tok // experts
    scale = 1.0 / math.sqrt(2 * topk * tok)
    pair_bit = lax.axis_size("section").bit_length() - 2
    rows = experts * cap

    own_gate = w_gate[0, 0]
    own_up = w_up[0, 0]
    own_down = w_down[0, 0]
    half = own_gate.shape[1]
    other_gate, other_up, other_down = partner((own_gate, own_up, own_down), "section", pair_bit)

    hit = dispatch_matrix(ids, cap, experts)
    pair_gate = jnp.sum(jnp.where(hit, gates.reshape(tok * topk)[None, :], 0.0), axis=1)
    sel = hit.reshape(rows, tok, topk).any(axis=2).astype(jnp.bfloat16)
    both = jnp.concatenate([inputs, grads], axis=1)
    picked = jnp.dot(sel, both, preferred_element_type=jnp.float32)
    slot_in = picked[:, :width].astype(jnp.bfloat16)
    slot_grad = (picked[:, width:] * pair_gate[:, None]).astype(jnp.bfloat16)
    send = jnp.concatenate([slot_in, slot_grad], axis=1).reshape(experts, cap, 2 * width)
    recv = lax.all_to_all(send, "expert", split_axis=0, concat_axis=0, tiled=True)
    sel_t = lax.optimization_barrier(
        jnp.transpose(hit.reshape(rows, tok, topk).any(axis=2)).astype(jnp.bfloat16)
    )
    recv = recv.reshape(rows, 2 * width)

    full_gate = jnp.concatenate([own_gate, other_gate], axis=1)
    full_up = jnp.concatenate([own_up, other_up], axis=1)
    full_down = jnp.concatenate([own_down, other_down], axis=0)
    pair_grad, grad_g, grad_u, grad_d = expert_grads(
        recv[:, :width], recv[:, width:], full_gate, full_up, full_down
    )
    back = pair_grad.astype(jnp.bfloat16).reshape(experts, cap, width)
    home = lax.all_to_all(back, "expert", split_axis=0, concat_axis=0, tiled=True)
    peer_g, peer_u, peer_d = partner(
        (
            grad_g[:, half:].astype(jnp.bfloat16),
            grad_u[:, half:].astype(jnp.bfloat16),
            grad_d[half:, :].astype(jnp.bfloat16),
        ),
        "section",
        pair_bit,
    )
    token_acc = jnp.dot(sel_t, home.reshape(rows, width), preferred_element_type=jnp.float32)
    mine_g = grad_g[:, :half] + peer_g.astype(jnp.float32)
    mine_u = grad_u[:, :half] + peer_u.astype(jnp.float32)
    mine_d = grad_d[:half, :] + peer_d.astype(jnp.float32)
    token_grad = token_acc.astype(jnp.bfloat16)
    out_g = (mine_g * scale).astype(jnp.bfloat16)
    out_u = (mine_u * scale).astype(jnp.bfloat16)
    out_d = (mine_d * scale).astype(jnp.bfloat16)
    return (token_grad[None], out_g[None, None], out_u[None, None], out_d[None, None])


def solution(mesh):
    in_specs = (
        P("section", "expert", None),
        P("section", "expert", None),
        P("section", "expert", None),
        P("section", "expert", None),
        P("section", "expert", None, None),
        P("section", "expert", None, None),
        P("section", "expert", None, None),
    )
    out_specs = (
        P("section", "expert", None),
        P("section", "expert", None, None),
        P("section", "expert", None, None),
        P("section", "expert", None, None),
    )
    return jax.shard_map(per_device, mesh=mesh, in_specs=in_specs, out_specs=out_specs, check_vma=False)
```

```python
import math

import jax
import jax.numpy as jnp
from jax import lax
from jax.sharding import PartitionSpec as P


def partner(value, axis, bit):
    mask = 2**bit
    pairs = [(source, source ^ mask) for source in range(lax.axis_size(axis))]
    return lax.ppermute(value, axis, pairs)


def dispatch_matrix(ids, cap, experts):
    tok, topk = ids.shape
    count = tok * topk
    flat = ids.reshape(count)
    onehot = (flat[:, None] == jnp.arange(experts, dtype=jnp.int32)[None, :]).astype(jnp.int32)
    before = jnp.cumsum(onehot, axis=0) - onehot
    rank = jnp.sum(before * onehot, axis=1)
    slot = flat * cap + rank
    hit = slot[None, :] == jnp.arange(experts * cap, dtype=jnp.int32)[:, None]
    return hit


def per_device(tokens, out_grad, expert_ids, gate_weights, w_gate, w_up, w_down):
    inputs = tokens[0]
    grads = out_grad[0]
    ids = expert_ids[0]
    gates = gate_weights[0]
    tok, topk = ids.shape
    width = inputs.shape[1]
    experts = lax.axis_size("expert")
    cap = 2 * topk * tok // experts
    scale = 1.0 / math.sqrt(2 * topk * tok)
    pair_bit = lax.axis_size("section").bit_length() - 2
    rows = experts * cap

    own_gate = w_gate[0, 0]
    own_up = w_up[0, 0]
    own_down = w_down[0, 0]
    half = own_gate.shape[1]
    other_gate, other_up, other_down = partner((own_gate, own_up, own_down), "section", pair_bit)

    hit = dispatch_matrix(ids, cap, experts)
    pair_gate = jnp.sum(jnp.where(hit, gates.reshape(tok * topk)[None, :], 0.0), axis=1)
    sel = hit.reshape(rows, tok, topk).any(axis=2).astype(jnp.bfloat16)
    both = jnp.concatenate([inputs, grads], axis=1)
    picked = jnp.dot(sel, both, preferred_element_type=jnp.float32)
    slot_in = picked[:, :width].astype(jnp.bfloat16)
    slot_grad = (picked[:, width:] * pair_gate[:, None]).astype(jnp.bfloat16)
    send = jnp.concatenate([slot_in, slot_grad], axis=1).reshape(experts, cap, 2 * width)
    recv = lax.all_to_all(send, "expert", split_axis=0, concat_axis=0, tiled=True)
    sel_t = lax.optimization_barrier(
        jnp.transpose(hit.reshape(rows, tok, topk).any(axis=2)).astype(jnp.bfloat16)
    )
    recv = recv.reshape(rows, 2 * width)

    full_gu = jnp.concatenate([own_gate, other_gate, own_up, other_up], axis=1)
    full_down = jnp.concatenate([own_down, other_down], axis=0)
    rows_in = recv[:, :width]
    rows_grad = recv[:, width:]
    hidden = 2 * half
    contract_last = (((1,), (1,)), ((), ()))
    contract_rows = (((0,), (0,)), ((), ()))
    gu_pre = jnp.dot(rows_in, full_gu, preferred_element_type=jnp.float32)
    gate_pre = gu_pre[:, :hidden]
    up_pre = gu_pre[:, hidden:]
    sigmoid_g = jax.nn.sigmoid(gate_pre)
    swish_val = gate_pre * sigmoid_g
    act = (swish_val * up_pre).astype(jnp.bfloat16)
    act_grad = lax.dot_general(rows_grad, full_down, contract_last, preferred_element_type=jnp.float32)
    gate_grad = (act_grad * up_pre * sigmoid_g * (1.0 + gate_pre * (1.0 - sigmoid_g))).astype(
        jnp.bfloat16
    )
    up_grad = (act_grad * swish_val).astype(jnp.bfloat16)
    gu_grad = jnp.concatenate([gate_grad, up_grad], axis=1)
    pair_grad = lax.dot_general(gu_grad, full_gu, contract_last, preferred_element_type=jnp.float32)
    back = pair_grad.astype(jnp.bfloat16).reshape(experts, cap, width)
    home = lax.all_to_all(back, "expert", split_axis=0, concat_axis=0, tiled=True)
    grad_gu = lax.dot_general(rows_in, gu_grad, contract_rows, preferred_element_type=jnp.float32)
    grad_d = lax.dot_general(act, rows_grad, contract_rows, preferred_element_type=jnp.float32)
    split_gu = grad_gu.reshape(width, 2, 2, half)
    peer_gu, peer_d = partner(
        (split_gu[:, :, 1, :].astype(jnp.bfloat16), grad_d[half:, :].astype(jnp.bfloat16)),
        "section",
        pair_bit,
    )
    token_acc = jnp.dot(sel_t, home.reshape(rows, width), preferred_element_type=jnp.float32)
    mine_g = split_gu[:, 0, 0, :] + peer_gu[:, 0, :].astype(jnp.float32)
    mine_u = split_gu[:, 1, 0, :] + peer_gu[:, 1, :].astype(jnp.float32)
    mine_d = grad_d[:half, :] + peer_d.astype(jnp.float32)
    token_grad = token_acc.astype(jnp.bfloat16)
    out_g = (mine_g * scale).astype(jnp.bfloat16)
    out_u = (mine_u * scale).astype(jnp.bfloat16)
    out_d = (mine_d * scale).astype(jnp.bfloat16)
    return (token_grad[None], out_g[None, None], out_u[None, None], out_d[None, None])


def solution(mesh):
    in_specs = (
        P("section", "expert", None),
        P("section", "expert", None),
        P("section", "expert", None),
        P("section", "expert", None),
        P("section", "expert", None, None),
        P("section", "expert", None, None),
        P("section", "expert", None, None),
    )
    out_specs = (
        P("section", "expert", None),
        P("section", "expert", None, None),
        P("section", "expert", None, None),
        P("section", "expert", None, None),
    )
    return jax.shard_map(per_device, mesh=mesh, in_specs=in_specs, out_specs=out_specs, check_vma=False)
```

```python
import math

import jax
import jax.numpy as jnp
from jax import lax
from jax.sharding import PartitionSpec as P


def partner(value, axis, bit):
    mask = 2**bit
    pairs = [(source, source ^ mask) for source in range(lax.axis_size(axis))]
    return lax.ppermute(value, axis, pairs)


def dispatch_matrix(ids, cap, experts):
    tok, topk = ids.shape
    count = tok * topk
    flat = ids.reshape(count)
    onehot = (flat[:, None] == jnp.arange(experts, dtype=jnp.int32)[None, :]).astype(jnp.int32)
    before = jnp.cumsum(onehot, axis=0) - onehot
    rank = jnp.sum(before * onehot, axis=1)
    slot = flat * cap + rank
    hit = slot[None, :] == jnp.arange(experts * cap, dtype=jnp.int32)[:, None]
    return hit


def per_device(tokens, out_grad, expert_ids, gate_weights, w_gate, w_up, w_down):
    inputs = tokens[0]
    grads = out_grad[0]
    ids = expert_ids[0]
    gates = gate_weights[0]
    tok, topk = ids.shape
    width = inputs.shape[1]
    experts = lax.axis_size("expert")
    cap = 2 * topk * tok // experts
    scale = 1.0 / math.sqrt(2 * topk * tok)
    pair_bit = lax.axis_size("section").bit_length() - 2
    rows = experts * cap

    own_gate = w_gate[0, 0]
    own_up = w_up[0, 0]
    own_down = w_down[0, 0]
    half = own_gate.shape[1]
    other_gate, other_up, other_down = partner((own_gate, own_up, own_down), "section", pair_bit)

    hit = dispatch_matrix(ids, cap, experts)
    pair_gate = jnp.sum(jnp.where(hit, gates.reshape(tok * topk)[None, :], 0.0), axis=1)
    sel = hit.reshape(rows, tok, topk).any(axis=2).astype(jnp.bfloat16)
    both = jnp.concatenate([inputs, grads], axis=1)
    picked = jnp.dot(sel, both, preferred_element_type=jnp.float32)
    slot_in = picked[:, :width].astype(jnp.bfloat16)
    slot_grad = (picked[:, width:] * pair_gate[:, None]).astype(jnp.bfloat16)
    send = jnp.concatenate([slot_in, slot_grad], axis=1).reshape(experts, cap, 2 * width)
    recv = lax.all_to_all(send, "expert", split_axis=0, concat_axis=0, tiled=True)
    sel_t = lax.optimization_barrier(
        jnp.transpose(hit.reshape(rows, tok, topk).any(axis=2)).astype(jnp.bfloat16)
    )
    recv = recv.reshape(rows, 2 * width)

    full_gu = jnp.concatenate([own_gate, other_gate, own_up, other_up], axis=1)
    full_down = jnp.concatenate([own_down, other_down], axis=0)
    rows_in = recv[:, :width]
    rows_grad = recv[:, width:]
    hidden = 2 * half
    contract_last = (((1,), (1,)), ((), ()))
    contract_rows = (((0,), (0,)), ((), ()))
    gu_pre = jnp.dot(rows_in, full_gu, preferred_element_type=jnp.float32)
    gate_pre = gu_pre[:, :hidden]
    up_pre = gu_pre[:, hidden:]
    sigmoid_g = jax.nn.sigmoid(gate_pre)
    swish_val = gate_pre * sigmoid_g
    act = (swish_val * up_pre).astype(jnp.bfloat16)
    act_grad = lax.dot_general(rows_grad, full_down, contract_last, preferred_element_type=jnp.float32)
    gate_grad = (act_grad * up_pre * sigmoid_g * (1.0 + gate_pre * (1.0 - sigmoid_g))).astype(
        jnp.bfloat16
    )
    up_grad = (act_grad * swish_val).astype(jnp.bfloat16)
    gu_grad = jnp.concatenate([gate_grad, up_grad], axis=1)
    pair_grad = lax.dot_general(gu_grad, full_gu, contract_last, preferred_element_type=jnp.float32)
    back = pair_grad.astype(jnp.bfloat16).reshape(experts, cap, width)
    home = lax.all_to_all(back, "expert", split_axis=0, concat_axis=0, tiled=True)
    grad_gu = lax.dot_general(rows_in, gu_grad, contract_rows, preferred_element_type=jnp.float32)
    grad_d = lax.dot_general(act, rows_grad, contract_rows, preferred_element_type=jnp.float32)
    peer_g, peer_u, peer_d = partner(
        (
            grad_gu[:, half:hidden].astype(jnp.bfloat16),
            grad_gu[:, hidden + half:].astype(jnp.bfloat16),
            grad_d[half:, :].astype(jnp.bfloat16),
        ),
        "section",
        pair_bit,
    )
    token_acc = jnp.dot(sel_t, home.reshape(rows, width), preferred_element_type=jnp.float32)
    mine_g = grad_gu[:, :half] + peer_g.astype(jnp.float32)
    mine_u = grad_gu[:, hidden:hidden + half] + peer_u.astype(jnp.float32)
    mine_d = grad_d[:half, :] + peer_d.astype(jnp.float32)
    token_grad = token_acc.astype(jnp.bfloat16)
    out_g = (mine_g * scale).astype(jnp.bfloat16)
    out_u = (mine_u * scale).astype(jnp.bfloat16)
    out_d = (mine_d * scale).astype(jnp.bfloat16)
    return (token_grad[None], out_g[None, None], out_u[None, None], out_d[None, None])


def solution(mesh):
    in_specs = (
        P("section", "expert", None),
        P("section", "expert", None),
        P("section", "expert", None),
        P("section", "expert", None),
        P("section", "expert", None, None),
        P("section", "expert", None, None),
        P("section", "expert", None, None),
    )
    out_specs = (
        P("section", "expert", None),
        P("section", "expert", None, None),
        P("section", "expert", None, None),
        P("section", "expert", None, None),
    )
    return jax.shard_map(per_device, mesh=mesh, in_specs=in_specs, out_specs=out_specs, check_vma=False)
```

```python
import math

import jax
import jax.numpy as jnp
from jax import lax
from jax.sharding import PartitionSpec as P


def partner(value, axis, bit):
    mask = 2**bit
    pairs = [(source, source ^ mask) for source in range(lax.axis_size(axis))]
    return lax.ppermute(value, axis, pairs)


def dispatch_matrix(ids, cap, experts):
    tok, topk = ids.shape
    count = tok * topk
    flat = ids.reshape(count)
    onehot = (flat[:, None] == jnp.arange(experts, dtype=jnp.int32)[None, :]).astype(jnp.int32)
    before = jnp.cumsum(onehot, axis=0) - onehot
    rank = jnp.sum(before * onehot, axis=1)
    slot = flat * cap + rank
    hit = slot[None, :] == jnp.arange(experts * cap, dtype=jnp.int32)[:, None]
    return hit


def per_device(tokens, out_grad, expert_ids, gate_weights, w_gate, w_up, w_down):
    inputs = tokens[0]
    grads = out_grad[0]
    ids = expert_ids[0]
    gates = gate_weights[0]
    tok, topk = ids.shape
    width = inputs.shape[1]
    experts = lax.axis_size("expert")
    cap = 2 * topk * tok // experts
    scale = 1.0 / math.sqrt(2 * topk * tok)
    pair_bit = lax.axis_size("section").bit_length() - 2
    rows = experts * cap

    own_gate = w_gate[0, 0]
    own_up = w_up[0, 0]
    own_down = w_down[0, 0]
    half = own_gate.shape[1]
    other_gate, other_up, other_down = partner((own_gate, own_up, own_down), "section", pair_bit)

    hit = dispatch_matrix(ids, cap, experts)
    pair_gate = jnp.sum(jnp.where(hit, gates.reshape(tok * topk)[None, :], 0.0), axis=1)
    sel = hit.reshape(rows, tok, topk).any(axis=2).astype(jnp.bfloat16)
    both = jnp.concatenate([inputs, grads], axis=1)
    picked = jnp.dot(sel, both, preferred_element_type=jnp.float32)
    slot_in = picked[:, :width].astype(jnp.bfloat16)
    slot_grad = (picked[:, width:] * pair_gate[:, None]).astype(jnp.bfloat16)
    send = jnp.concatenate([slot_in, slot_grad], axis=1).reshape(experts, cap, 2 * width)
    recv = lax.all_to_all(send, "expert", split_axis=0, concat_axis=0, tiled=True)
    sel_t = lax.optimization_barrier(
        jnp.transpose(hit.reshape(rows, tok, topk).any(axis=2)).astype(jnp.bfloat16)
    )
    recv = recv.reshape(rows, 2 * width)

    full_gu = jnp.concatenate([own_gate, other_gate, own_up, other_up], axis=1)
    full_down = jnp.concatenate([own_down, other_down], axis=0)
    rows_in = recv[:, :width]
    rows_grad = recv[:, width:]
    hidden = 2 * half
    contract_last = (((1,), (1,)), ((), ()))
    contract_rows = (((0,), (0,)), ((), ()))
    gu_pre = jnp.dot(rows_in, full_gu, preferred_element_type=jnp.float32)
    gate_pre = gu_pre[:, :hidden]
    up_pre = gu_pre[:, hidden:]
    sigmoid_g = jax.nn.sigmoid(gate_pre)
    swish_val = gate_pre * sigmoid_g
    act = (swish_val * up_pre).astype(jnp.bfloat16)
    act_grad = lax.dot_general(rows_grad, full_down, contract_last, preferred_element_type=jnp.float32)
    gate_grad = (act_grad * up_pre * sigmoid_g * (1.0 + gate_pre * (1.0 - sigmoid_g))).astype(
        jnp.bfloat16
    )
    up_grad = (act_grad * swish_val).astype(jnp.bfloat16)
    gu_grad = jnp.concatenate([gate_grad, up_grad], axis=1)
    pair_grad = lax.dot_general(gu_grad, full_gu, contract_last, preferred_element_type=jnp.float32)
    back = pair_grad.astype(jnp.bfloat16).reshape(experts, cap, width)
    home = lax.all_to_all(back, "expert", split_axis=0, concat_axis=0, tiled=True)
    def grad_cols(lo, hi):
        return (
            lax.dot_general(rows_in, gate_grad[:, lo:hi], contract_rows, preferred_element_type=jnp.float32),
            lax.dot_general(rows_in, up_grad[:, lo:hi], contract_rows, preferred_element_type=jnp.float32),
            lax.dot_general(act[:, lo:hi], rows_grad, contract_rows, preferred_element_type=jnp.float32),
        )

    peer_terms = grad_cols(half, hidden)
    peer_g, peer_u, peer_d = partner(
        tuple(t.astype(jnp.bfloat16) for t in peer_terms), "section", pair_bit
    )
    own_g, own_u, own_d = grad_cols(0, half)
    token_acc = jnp.dot(sel_t, home.reshape(rows, width), preferred_element_type=jnp.float32)
    mine_g = own_g + peer_g.astype(jnp.float32)
    mine_u = own_u + peer_u.astype(jnp.float32)
    mine_d = own_d + peer_d.astype(jnp.float32)
    token_grad = token_acc.astype(jnp.bfloat16)
    out_g = (mine_g * scale).astype(jnp.bfloat16)
    out_u = (mine_u * scale).astype(jnp.bfloat16)
    out_d = (mine_d * scale).astype(jnp.bfloat16)
    return (token_grad[None], out_g[None, None], out_u[None, None], out_d[None, None])


def solution(mesh):
    in_specs = (
        P("section", "expert", None),
        P("section", "expert", None),
        P("section", "expert", None),
        P("section", "expert", None),
        P("section", "expert", None, None),
        P("section", "expert", None, None),
        P("section", "expert", None, None),
    )
    out_specs = (
        P("section", "expert", None),
        P("section", "expert", None, None),
        P("section", "expert", None, None),
        P("section", "expert", None, None),
    )
    return jax.shard_map(per_device, mesh=mesh, in_specs=in_specs, out_specs=out_specs, check_vma=False)
```

```python
import math

import jax
import jax.numpy as jnp
from jax import lax
from jax.sharding import PartitionSpec as P


def partner(value, axis, bit):
    mask = 2**bit
    pairs = [(source, source ^ mask) for source in range(lax.axis_size(axis))]
    return lax.ppermute(value, axis, pairs)


def dispatch_matrix(ids, cap, experts):
    tok, topk = ids.shape
    count = tok * topk
    flat = ids.reshape(count)
    onehot = (flat[:, None] == jnp.arange(experts, dtype=jnp.int32)[None, :]).astype(jnp.int32)
    before = jnp.cumsum(onehot, axis=0) - onehot
    rank = jnp.sum(before * onehot, axis=1)
    slot = flat * cap + rank
    hit = slot[None, :] == jnp.arange(experts * cap, dtype=jnp.int32)[:, None]
    return hit


def per_device(tokens, out_grad, expert_ids, gate_weights, w_gate, w_up, w_down):
    inputs = tokens[0]
    grads = out_grad[0]
    ids = expert_ids[0]
    gates = gate_weights[0]
    tok, topk = ids.shape
    width = inputs.shape[1]
    experts = lax.axis_size("expert")
    cap = 2 * topk * tok // experts
    scale = 1.0 / math.sqrt(2 * topk * tok)
    pair_bit = lax.axis_size("section").bit_length() - 2
    rows = experts * cap

    own_gate = w_gate[0, 0]
    own_up = w_up[0, 0]
    own_down = w_down[0, 0]
    half = own_gate.shape[1]
    other_gate, other_up, other_down = partner((own_gate, own_up, own_down), "section", pair_bit)

    hit = dispatch_matrix(ids, cap, experts)
    pair_gate = jnp.sum(jnp.where(hit, gates.reshape(tok * topk)[None, :], 0.0), axis=1)
    sel = hit.reshape(rows, tok, topk).any(axis=2).astype(jnp.bfloat16)
    both = jnp.concatenate([inputs, grads], axis=1)
    picked = jnp.dot(sel, both, preferred_element_type=jnp.bfloat16)
    slot_in = picked[:, :width]
    slot_grad = (picked[:, width:].astype(jnp.float32) * pair_gate[:, None]).astype(jnp.bfloat16)
    send = jnp.concatenate([slot_in, slot_grad], axis=1).reshape(experts, cap, 2 * width)
    recv = lax.all_to_all(send, "expert", split_axis=0, concat_axis=0, tiled=True)
    sel_t = lax.optimization_barrier(
        jnp.transpose(hit.reshape(rows, tok, topk).any(axis=2)).astype(jnp.bfloat16)
    )
    recv = recv.reshape(rows, 2 * width)

    full_gu = jnp.concatenate([own_gate, other_gate, own_up, other_up], axis=1)
    full_down = jnp.concatenate([own_down, other_down], axis=0)
    rows_in = recv[:, :width]
    rows_grad = recv[:, width:]
    hidden = 2 * half
    contract_last = (((1,), (1,)), ((), ()))
    contract_rows = (((0,), (0,)), ((), ()))
    gu_pre = jnp.dot(rows_in, full_gu, preferred_element_type=jnp.float32)
    gate_pre = gu_pre[:, :hidden]
    up_pre = gu_pre[:, hidden:]
    sigmoid_g = jax.nn.sigmoid(gate_pre)
    swish_val = gate_pre * sigmoid_g
    act = (swish_val * up_pre).astype(jnp.bfloat16)
    act_grad = lax.dot_general(rows_grad, full_down, contract_last, preferred_element_type=jnp.float32)
    gate_grad = (act_grad * up_pre * sigmoid_g * (1.0 + gate_pre * (1.0 - sigmoid_g))).astype(
        jnp.bfloat16
    )
    up_grad = (act_grad * swish_val).astype(jnp.bfloat16)
    gu_grad = jnp.concatenate([gate_grad, up_grad], axis=1)
    pair_grad = lax.dot_general(gu_grad, full_gu, contract_last, preferred_element_type=jnp.float32)
    back = pair_grad.astype(jnp.bfloat16).reshape(experts, cap, width)
    home = lax.all_to_all(back, "expert", split_axis=0, concat_axis=0, tiled=True)
    def grad_cols(lo, hi):
        return (
            lax.dot_general(rows_in, gate_grad[:, lo:hi], contract_rows, preferred_element_type=jnp.float32),
            lax.dot_general(rows_in, up_grad[:, lo:hi], contract_rows, preferred_element_type=jnp.float32),
            lax.dot_general(act[:, lo:hi], rows_grad, contract_rows, preferred_element_type=jnp.float32),
        )

    peer_terms = grad_cols(half, hidden)
    peer_g, peer_u, peer_d = partner(
        tuple(t.astype(jnp.bfloat16) for t in peer_terms), "section", pair_bit
    )
    own_g, own_u, own_d = grad_cols(0, half)
    token_acc = jnp.dot(sel_t, home.reshape(rows, width), preferred_element_type=jnp.float32)
    mine_g = own_g + peer_g.astype(jnp.float32)
    mine_u = own_u + peer_u.astype(jnp.float32)
    mine_d = own_d + peer_d.astype(jnp.float32)
    token_grad = token_acc.astype(jnp.bfloat16)
    out_g = (mine_g * scale).astype(jnp.bfloat16)
    out_u = (mine_u * scale).astype(jnp.bfloat16)
    out_d = (mine_d * scale).astype(jnp.bfloat16)
    return (token_grad[None], out_g[None, None], out_u[None, None], out_d[None, None])


def solution(mesh):
    in_specs = (
        P("section", "expert", None),
        P("section", "expert", None),
        P("section", "expert", None),
        P("section", "expert", None),
        P("section", "expert", None, None),
        P("section", "expert", None, None),
        P("section", "expert", None, None),
    )
    out_specs = (
        P("section", "expert", None),
        P("section", "expert", None, None),
        P("section", "expert", None, None),
        P("section", "expert", None, None),
    )
    return jax.shard_map(per_device, mesh=mesh, in_specs=in_specs, out_specs=out_specs, check_vma=False)
```

```python
import math

import jax
import jax.numpy as jnp
from jax import lax
from jax.sharding import PartitionSpec as P


def partner(value, axis, bit):
    mask = 2**bit
    pairs = [(source, source ^ mask) for source in range(lax.axis_size(axis))]
    return lax.ppermute(value, axis, pairs)


def dispatch_matrix(ids, cap, experts):
    tok, topk = ids.shape
    count = tok * topk
    flat = ids.reshape(count)
    onehot = (flat[:, None] == jnp.arange(experts, dtype=jnp.int32)[None, :]).astype(jnp.int32)
    before = jnp.cumsum(onehot, axis=0) - onehot
    rank = jnp.sum(before * onehot, axis=1)
    slot = flat * cap + rank
    hit = slot[None, :] == jnp.arange(experts * cap, dtype=jnp.int32)[:, None]
    return hit


def per_device(tokens, out_grad, expert_ids, gate_weights, w_gate, w_up, w_down):
    inputs = tokens[0]
    grads = out_grad[0]
    ids = expert_ids[0]
    gates = gate_weights[0]
    tok, topk = ids.shape
    width = inputs.shape[1]
    experts = lax.axis_size("expert")
    cap = 2 * topk * tok // experts
    scale = 1.0 / math.sqrt(2 * topk * tok)
    pair_bit = lax.axis_size("section").bit_length() - 2
    rows = experts * cap

    own_gate = w_gate[0, 0]
    own_up = w_up[0, 0]
    own_down = w_down[0, 0]
    half = own_gate.shape[1]
    other_gate, other_up, other_down = partner((own_gate, own_up, own_down), "section", pair_bit)

    hit = dispatch_matrix(ids, cap, experts)
    pair_gate = jnp.sum(jnp.where(hit, gates.reshape(tok * topk)[None, :], 0.0), axis=1)
    sel = hit.reshape(rows, tok, topk).any(axis=2).astype(jnp.bfloat16)
    both = jnp.concatenate([inputs, grads], axis=1)
    picked = jnp.dot(sel, both, preferred_element_type=jnp.float32)
    slot_in = picked[:, :width].astype(jnp.bfloat16)
    slot_grad = (picked[:, width:] * pair_gate[:, None]).astype(jnp.bfloat16)
    send = jnp.concatenate([slot_in, slot_grad], axis=1).reshape(experts, cap, 2 * width)
    tail = cap // 4
    recv1 = lax.all_to_all(send[:, :tail], "expert", split_axis=0, concat_axis=0, tiled=True)
    recv0 = lax.all_to_all(send[:, tail:], "expert", split_axis=0, concat_axis=0, tiled=True)
    sel_t = lax.optimization_barrier(
        jnp.transpose(hit.reshape(rows, tok, topk).any(axis=2)).astype(jnp.bfloat16)
    )

    full_gu = jnp.concatenate([own_gate, other_gate, own_up, other_up], axis=1)
    full_down = jnp.concatenate([own_down, other_down], axis=0)
    hidden = 2 * half
    contract_last = (((1,), (1,)), ((), ()))
    contract_rows = (((0,), (0,)), ((), ()))

    def chunk(recv_part):
        part = recv_part.reshape(-1, 2 * width)
        rows_in = part[:, :width]
        rows_grad = part[:, width:]
        gu_pre = jnp.dot(rows_in, full_gu, preferred_element_type=jnp.float32)
        gate_pre = gu_pre[:, :hidden]
        up_pre = gu_pre[:, hidden:]
        sigmoid_g = jax.nn.sigmoid(gate_pre)
        swish_val = gate_pre * sigmoid_g
        act = (swish_val * up_pre).astype(jnp.bfloat16)
        act_grad = lax.dot_general(
            rows_grad, full_down, contract_last, preferred_element_type=jnp.float32
        )
        gate_grad = (act_grad * up_pre * sigmoid_g * (1.0 + gate_pre * (1.0 - sigmoid_g))).astype(
            jnp.bfloat16
        )
        up_grad = (act_grad * swish_val).astype(jnp.bfloat16)
        gu_grad = jnp.concatenate([gate_grad, up_grad], axis=1)
        pair_grad = lax.dot_general(
            gu_grad, full_gu, contract_last, preferred_element_type=jnp.float32
        )
        return rows_in, rows_grad, gate_grad, up_grad, act, pair_grad.astype(jnp.bfloat16)

    c0 = chunk(recv0)
    c1 = chunk(recv1)
    back = jnp.concatenate(
        [c1[5].reshape(experts, tail, width), c0[5].reshape(experts, cap - tail, width)], axis=1
    )
    home = lax.all_to_all(back, "expert", split_axis=0, concat_axis=0, tiled=True)

    def grad_cols(lo, hi):
        total = None
        for rows_in, rows_grad, gate_grad, up_grad, act, _ in (c0, c1):
            terms = (
                lax.dot_general(rows_in, gate_grad[:, lo:hi], contract_rows, preferred_element_type=jnp.float32),
                lax.dot_general(rows_in, up_grad[:, lo:hi], contract_rows, preferred_element_type=jnp.float32),
                lax.dot_general(act[:, lo:hi], rows_grad, contract_rows, preferred_element_type=jnp.float32),
            )
            total = terms if total is None else tuple(x + y for x, y in zip(total, terms))
        return total

    peer_terms = grad_cols(half, hidden)
    peer_g, peer_u, peer_d = partner(
        tuple(t.astype(jnp.bfloat16) for t in peer_terms), "section", pair_bit
    )
    own_g, own_u, own_d = grad_cols(0, half)
    token_acc = jnp.dot(sel_t, home.reshape(rows, width), preferred_element_type=jnp.float32)
    mine_g = own_g + peer_g.astype(jnp.float32)
    mine_u = own_u + peer_u.astype(jnp.float32)
    mine_d = own_d + peer_d.astype(jnp.float32)
    token_grad = token_acc.astype(jnp.bfloat16)
    out_g = (mine_g * scale).astype(jnp.bfloat16)
    out_u = (mine_u * scale).astype(jnp.bfloat16)
    out_d = (mine_d * scale).astype(jnp.bfloat16)
    return (token_grad[None], out_g[None, None], out_u[None, None], out_d[None, None])


def solution(mesh):
    in_specs = (
        P("section", "expert", None),
        P("section", "expert", None),
        P("section", "expert", None),
        P("section", "expert", None),
        P("section", "expert", None, None),
        P("section", "expert", None, None),
        P("section", "expert", None, None),
    )
    out_specs = (
        P("section", "expert", None),
        P("section", "expert", None, None),
        P("section", "expert", None, None),
        P("section", "expert", None, None),
    )
    return jax.shard_map(per_device, mesh=mesh, in_specs=in_specs, out_specs=out_specs, check_vma=False)
```

```python
import math

import jax
import jax.numpy as jnp
from jax import lax
from jax.sharding import PartitionSpec as P


def partner(value, axis, bit):
    mask = 2**bit
    pairs = [(source, source ^ mask) for source in range(lax.axis_size(axis))]
    return lax.ppermute(value, axis, pairs)


def dispatch_matrix(ids, cap, experts):
    tok, topk = ids.shape
    count = tok * topk
    flat = ids.reshape(count)
    onehot = (flat[:, None] == jnp.arange(experts, dtype=jnp.int32)[None, :]).astype(jnp.int32)
    before = jnp.cumsum(onehot, axis=0) - onehot
    rank = jnp.sum(before * onehot, axis=1)
    slot = flat * cap + rank
    hit = slot[None, :] == jnp.arange(experts * cap, dtype=jnp.int32)[:, None]
    return hit


def per_device(tokens, out_grad, expert_ids, gate_weights, w_gate, w_up, w_down):
    inputs = tokens[0]
    grads = out_grad[0]
    ids = expert_ids[0]
    gates = gate_weights[0]
    tok, topk = ids.shape
    width = inputs.shape[1]
    experts = lax.axis_size("expert")
    cap = 2 * topk * tok // experts
    scale = 1.0 / math.sqrt(2 * topk * tok)
    pair_bit = lax.axis_size("section").bit_length() - 2
    rows = experts * cap

    own_gate = w_gate[0, 0]
    own_up = w_up[0, 0]
    own_down = w_down[0, 0]
    half = own_gate.shape[1]
    other_gate, other_up, other_down = partner((own_gate, own_up, own_down), "section", pair_bit)

    hit = dispatch_matrix(ids, cap, experts)
    pair_gate = jnp.sum(jnp.where(hit, gates.reshape(tok * topk)[None, :], 0.0), axis=1)
    sel = hit.reshape(rows, tok, topk).any(axis=2).astype(jnp.bfloat16)
    both = jnp.concatenate([inputs, grads], axis=1)
    picked = jnp.dot(sel, both, preferred_element_type=jnp.float32)
    slot_in = picked[:, :width].astype(jnp.bfloat16)
    slot_grad = (picked[:, width:] * pair_gate[:, None]).astype(jnp.bfloat16)
    send = jnp.concatenate([slot_in, slot_grad], axis=1).reshape(experts, cap, 2 * width)
    recv = lax.all_to_all(send, "expert", split_axis=0, concat_axis=0, tiled=True)
    sel_t = lax.optimization_barrier(
        jnp.transpose(hit.reshape(rows, tok, topk).any(axis=2)).astype(jnp.bfloat16)
    )
    recv = recv.reshape(rows, 2 * width)

    full_gu = jnp.concatenate([own_gate, other_gate, own_up, other_up], axis=1)
    full_down = jnp.concatenate([own_down, other_down], axis=0)
    rows_in = recv[:, :width]
    rows_grad = recv[:, width:]
    hidden = 2 * half
    contract_last = (((1,), (1,)), ((), ()))
    contract_rows = (((0,), (0,)), ((), ()))
    gu_pre = jnp.dot(rows_in, full_gu, preferred_element_type=jnp.float32)
    gate_pre = gu_pre[:, :hidden]
    up_pre = gu_pre[:, hidden:]
    sigmoid_g = jax.nn.sigmoid(gate_pre)
    swish_val = gate_pre * sigmoid_g
    act = (swish_val * up_pre).astype(jnp.bfloat16)
    act_grad = lax.dot_general(rows_grad, full_down, contract_last, preferred_element_type=jnp.float32)
    gate_grad = (act_grad * up_pre * sigmoid_g * (1.0 + gate_pre * (1.0 - sigmoid_g))).astype(
        jnp.bfloat16
    )
    up_grad = (act_grad * swish_val).astype(jnp.bfloat16)
    gu_grad = jnp.concatenate([gate_grad, up_grad], axis=1)
    pair_grad = lax.dot_general(gu_grad, full_gu, contract_last, preferred_element_type=jnp.float32)
    back = pair_grad.astype(jnp.bfloat16).reshape(experts, cap, width)
    home = lax.all_to_all(back, "expert", split_axis=0, concat_axis=0, tiled=True)
    def grad_cols(lo, hi):
        return (
            lax.dot_general(rows_in, gate_grad[:, lo:hi], contract_rows, preferred_element_type=jnp.float32),
            lax.dot_general(rows_in, up_grad[:, lo:hi], contract_rows, preferred_element_type=jnp.float32),
            lax.dot_general(act[:, lo:hi], rows_grad, contract_rows, preferred_element_type=jnp.float32),
        )

    peer_terms = grad_cols(half, hidden)
    peer_d = partner(peer_terms[2].astype(jnp.bfloat16), "section", pair_bit)
    peer_g, peer_u = partner(
        tuple(t.astype(jnp.bfloat16) for t in peer_terms[:2]), "section", pair_bit
    )
    own_g, own_u, own_d = grad_cols(0, half)
    token_acc = jnp.dot(sel_t, home.reshape(rows, width), preferred_element_type=jnp.float32)
    mine_g = own_g + peer_g.astype(jnp.float32)
    mine_u = own_u + peer_u.astype(jnp.float32)
    mine_d = own_d + peer_d.astype(jnp.float32)
    token_grad = token_acc.astype(jnp.bfloat16)
    out_g = (mine_g * scale).astype(jnp.bfloat16)
    out_u = (mine_u * scale).astype(jnp.bfloat16)
    out_d = (mine_d * scale).astype(jnp.bfloat16)
    return (token_grad[None], out_g[None, None], out_u[None, None], out_d[None, None])


def solution(mesh):
    in_specs = (
        P("section", "expert", None),
        P("section", "expert", None),
        P("section", "expert", None),
        P("section", "expert", None),
        P("section", "expert", None, None),
        P("section", "expert", None, None),
        P("section", "expert", None, None),
    )
    out_specs = (
        P("section", "expert", None),
        P("section", "expert", None, None),
        P("section", "expert", None, None),
        P("section", "expert", None, None),
    )
    return jax.shard_map(per_device, mesh=mesh, in_specs=in_specs, out_specs=out_specs, check_vma=False)
```

```python
import math

import jax
import jax.numpy as jnp
from jax import lax
from jax.sharding import PartitionSpec as P


def partner(value, axis, bit):
    mask = 2**bit
    pairs = [(source, source ^ mask) for source in range(lax.axis_size(axis))]
    return lax.ppermute(value, axis, pairs)


def dispatch_matrix(ids, cap, experts):
    tok, topk = ids.shape
    count = tok * topk
    flat = ids.reshape(count)
    onehot = (flat[:, None] == jnp.arange(experts, dtype=jnp.int32)[None, :]).astype(jnp.int32)
    before = jnp.cumsum(onehot, axis=0) - onehot
    rank = jnp.sum(before * onehot, axis=1)
    slot = flat * cap + rank
    hit = slot[None, :] == jnp.arange(experts * cap, dtype=jnp.int32)[:, None]
    return hit


def per_device(tokens, out_grad, expert_ids, gate_weights, w_gate, w_up, w_down):
    inputs = tokens[0]
    grads = out_grad[0]
    ids = expert_ids[0]
    gates = gate_weights[0]
    tok, topk = ids.shape
    width = inputs.shape[1]
    experts = lax.axis_size("expert")
    cap = 2 * topk * tok // experts
    scale = 1.0 / math.sqrt(2 * topk * tok)
    pair_bit = lax.axis_size("section").bit_length() - 2
    rows = experts * cap

    own_gate = w_gate[0, 0]
    own_up = w_up[0, 0]
    own_down = w_down[0, 0]
    half = own_gate.shape[1]
    other_gate, other_up, other_down = partner((own_gate, own_up, own_down), "section", pair_bit)

    hit = dispatch_matrix(ids, cap, experts)
    pair_gate = jnp.sum(jnp.where(hit, gates.reshape(tok * topk)[None, :], 0.0), axis=1)
    sel = hit.reshape(rows, tok, topk).any(axis=2).astype(jnp.bfloat16)
    both = jnp.concatenate([inputs, grads], axis=1)
    picked = jnp.dot(sel, both, preferred_element_type=jnp.float32)
    slot_in = picked[:, :width].astype(jnp.bfloat16)
    slot_grad = (picked[:, width:] * pair_gate[:, None]).astype(jnp.bfloat16)
    send = jnp.concatenate([slot_in, slot_grad], axis=1).reshape(experts, cap, 2 * width)
    recv = lax.all_to_all(send, "expert", split_axis=0, concat_axis=0, tiled=True)
    sel_t = lax.optimization_barrier(
        jnp.transpose(hit.reshape(rows, tok, topk).any(axis=2)).astype(jnp.bfloat16)
    )
    recv = recv.reshape(rows, 2 * width)

    full_gu = jnp.concatenate([own_gate, other_gate, own_up, other_up], axis=1)
    full_down = jnp.concatenate([own_down, other_down], axis=0)
    rows_in = recv[:, :width]
    rows_grad = recv[:, width:]
    hidden = 2 * half
    contract_last = (((1,), (1,)), ((), ()))
    contract_rows = (((0,), (0,)), ((), ()))
    gu_pre = jnp.dot(rows_in, full_gu, preferred_element_type=jnp.float32)
    gate_pre = gu_pre[:, :hidden]
    up_pre = gu_pre[:, hidden:]
    sigmoid_g = jax.nn.sigmoid(gate_pre)
    swish_val = gate_pre * sigmoid_g
    act = (swish_val * up_pre).astype(jnp.bfloat16)
    act_grad = lax.dot_general(rows_grad, full_down, contract_last, preferred_element_type=jnp.float32)
    gate_grad = (act_grad * up_pre * sigmoid_g * (1.0 + gate_pre * (1.0 - sigmoid_g))).astype(
        jnp.bfloat16
    )
    up_grad = (act_grad * swish_val).astype(jnp.bfloat16)
    gu_grad = jnp.concatenate([gate_grad, up_grad], axis=1)
    pair_grad = lax.dot_general(gu_grad, full_gu, contract_last, preferred_element_type=jnp.float32)
    back = pair_grad.astype(jnp.bfloat16).reshape(experts, cap, width)
    home = lax.all_to_all(back, "expert", split_axis=0, concat_axis=0, tiled=True)
    def grad_cols(lo, hi):
        return (
            lax.dot_general(rows_in, gate_grad[:, lo:hi], contract_rows, preferred_element_type=jnp.float32),
            lax.dot_general(rows_in, up_grad[:, lo:hi], contract_rows, preferred_element_type=jnp.float32),
            lax.dot_general(act[:, lo:hi], rows_grad, contract_rows, preferred_element_type=jnp.float32),
        )

    peer_d_send = lax.dot_general(
        act[:, half:hidden], rows_grad, contract_rows, preferred_element_type=jnp.float32
    ).astype(jnp.bfloat16)
    peer_terms = grad_cols(half, hidden)
    peer_d = partner(peer_d_send, "section", pair_bit)
    peer_g, peer_u = partner(
        tuple(t.astype(jnp.bfloat16) for t in peer_terms[:2]), "section", pair_bit
    )
    own_g, own_u, own_d = grad_cols(0, half)
    token_acc = jnp.dot(sel_t, home.reshape(rows, width), preferred_element_type=jnp.float32)
    mine_g = own_g + peer_g.astype(jnp.float32)
    mine_u = own_u + peer_u.astype(jnp.float32)
    mine_d = own_d + peer_d.astype(jnp.float32)
    token_grad = token_acc.astype(jnp.bfloat16)
    out_g = (mine_g * scale).astype(jnp.bfloat16)
    out_u = (mine_u * scale).astype(jnp.bfloat16)
    out_d = (mine_d * scale).astype(jnp.bfloat16)
    return (token_grad[None], out_g[None, None], out_u[None, None], out_d[None, None])


def solution(mesh):
    in_specs = (
        P("section", "expert", None),
        P("section", "expert", None),
        P("section", "expert", None),
        P("section", "expert", None),
        P("section", "expert", None, None),
        P("section", "expert", None, None),
        P("section", "expert", None, None),
    )
    out_specs = (
        P("section", "expert", None),
        P("section", "expert", None, None),
        P("section", "expert", None, None),
        P("section", "expert", None, None),
    )
    return jax.shard_map(per_device, mesh=mesh, in_specs=in_specs, out_specs=out_specs, check_vma=False)
```

```python
import math

import jax
import jax.numpy as jnp
from jax import lax
from jax.sharding import PartitionSpec as P


def partner(value, axis, bit):
    mask = 2**bit
    pairs = [(source, source ^ mask) for source in range(lax.axis_size(axis))]
    return lax.ppermute(value, axis, pairs)


def dispatch_matrix(ids, cap, experts):
    tok, topk = ids.shape
    count = tok * topk
    flat = ids.reshape(count)
    match = flat[:, None] == jnp.arange(experts, dtype=jnp.int32)[None, :]
    order = jnp.arange(count, dtype=jnp.int32)
    earlier = (order[None, :] < order[:, None]).astype(jnp.bfloat16)
    before = jnp.dot(earlier, match.astype(jnp.bfloat16), preferred_element_type=jnp.float32)
    rank = jnp.sum(jnp.where(match, before, 0.0), axis=1).astype(jnp.int32)
    slot = flat * cap + rank
    hit = slot[None, :] == jnp.arange(experts * cap, dtype=jnp.int32)[:, None]
    return hit


def per_device(tokens, out_grad, expert_ids, gate_weights, w_gate, w_up, w_down):
    inputs = tokens[0]
    grads = out_grad[0]
    ids = expert_ids[0]
    gates = gate_weights[0]
    tok, topk = ids.shape
    width = inputs.shape[1]
    experts = lax.axis_size("expert")
    cap = 2 * topk * tok // experts
    scale = 1.0 / math.sqrt(2 * topk * tok)
    pair_bit = lax.axis_size("section").bit_length() - 2
    rows = experts * cap

    own_gate = w_gate[0, 0]
    own_up = w_up[0, 0]
    own_down = w_down[0, 0]
    half = own_gate.shape[1]
    other_gate, other_up, other_down = partner((own_gate, own_up, own_down), "section", pair_bit)

    hit = dispatch_matrix(ids, cap, experts)
    pair_gate = jnp.sum(
        jnp.where(hit.reshape(rows, tok, topk), gates[None, :, :], 0.0), axis=(1, 2)
    )
    sel = hit.reshape(rows, tok, topk).any(axis=2).astype(jnp.bfloat16)
    both = jnp.concatenate([inputs, grads], axis=1)
    picked = jnp.dot(sel, both, preferred_element_type=jnp.float32)
    slot_in = picked[:, :width].astype(jnp.bfloat16)
    slot_grad = (picked[:, width:] * pair_gate[:, None]).astype(jnp.bfloat16)
    send = jnp.concatenate([slot_in, slot_grad], axis=1).reshape(experts, cap, 2 * width)
    recv = lax.all_to_all(send, "expert", split_axis=0, concat_axis=0, tiled=True)
    sel_t = lax.optimization_barrier(
        jnp.transpose(hit.reshape(rows, tok, topk).any(axis=2)).astype(jnp.bfloat16)
    )
    recv = recv.reshape(rows, 2 * width)

    full_gu = jnp.concatenate([own_gate, other_gate, own_up, other_up], axis=1)
    full_down = jnp.concatenate([own_down, other_down], axis=0)
    rows_in = recv[:, :width]
    rows_grad = recv[:, width:]
    hidden = 2 * half
    contract_last = (((1,), (1,)), ((), ()))
    contract_rows = (((0,), (0,)), ((), ()))
    gu_pre = jnp.dot(rows_in, full_gu, preferred_element_type=jnp.float32)
    gate_pre = gu_pre[:, :hidden]
    up_pre = gu_pre[:, hidden:]
    sigmoid_g = jax.nn.sigmoid(gate_pre)
    swish_val = gate_pre * sigmoid_g
    act = (swish_val * up_pre).astype(jnp.bfloat16)
    act_grad = lax.dot_general(rows_grad, full_down, contract_last, preferred_element_type=jnp.float32)
    gate_grad = (act_grad * up_pre * sigmoid_g * (1.0 + gate_pre * (1.0 - sigmoid_g))).astype(
        jnp.bfloat16
    )
    up_grad = (act_grad * swish_val).astype(jnp.bfloat16)
    gu_grad = jnp.concatenate([gate_grad, up_grad], axis=1)
    pair_grad = lax.dot_general(gu_grad, full_gu, contract_last, preferred_element_type=jnp.float32)
    back = pair_grad.astype(jnp.bfloat16).reshape(experts, cap, width)
    home = lax.all_to_all(back, "expert", split_axis=0, concat_axis=0, tiled=True)
    def grad_cols(lo, hi):
        return (
            lax.dot_general(rows_in, gate_grad[:, lo:hi], contract_rows, preferred_element_type=jnp.float32),
            lax.dot_general(rows_in, up_grad[:, lo:hi], contract_rows, preferred_element_type=jnp.float32),
            lax.dot_general(act[:, lo:hi], rows_grad, contract_rows, preferred_element_type=jnp.float32),
        )

    peer_terms = grad_cols(half, hidden)
    peer_d = partner(peer_terms[2].astype(jnp.bfloat16), "section", pair_bit)
    peer_g, peer_u = partner(
        tuple(t.astype(jnp.bfloat16) for t in peer_terms[:2]), "section", pair_bit
    )
    own_g, own_u, own_d = grad_cols(0, half)
    token_acc = jnp.dot(sel_t, home.reshape(rows, width), preferred_element_type=jnp.float32)
    mine_g = own_g + peer_g.astype(jnp.float32)
    mine_u = own_u + peer_u.astype(jnp.float32)
    mine_d = own_d + peer_d.astype(jnp.float32)
    token_grad = token_acc.astype(jnp.bfloat16)
    out_g = (mine_g * scale).astype(jnp.bfloat16)
    out_u = (mine_u * scale).astype(jnp.bfloat16)
    out_d = (mine_d * scale).astype(jnp.bfloat16)
    return (token_grad[None], out_g[None, None], out_u[None, None], out_d[None, None])


def solution(mesh):
    in_specs = (
        P("section", "expert", None),
        P("section", "expert", None),
        P("section", "expert", None),
        P("section", "expert", None),
        P("section", "expert", None, None),
        P("section", "expert", None, None),
        P("section", "expert", None, None),
    )
    out_specs = (
        P("section", "expert", None),
        P("section", "expert", None, None),
        P("section", "expert", None, None),
        P("section", "expert", None, None),
    )
    return jax.shard_map(per_device, mesh=mesh, in_specs=in_specs, out_specs=out_specs, check_vma=False)
```
